128 devices in a mesh: gx: 16 (over y_hi, z, core), gy: 8 (over x, y_lo).
Axes of the slice: x: 4, y: 4 (y_hi: 2, y_lo: 2; y = y_hi * 2 + y_lo), z: 4, core: 2. Of those that a mesh axis runs over, the one named last changes fastest.
Arguments:
- tokens_in: bfloat16 [2, 256, 256, 512], P(None, 'gx', 'gy'), may hold values from -80 to 80
- grad_out: bfloat16 [2, 256, 256, 512], P(None, 'gx', 'gy'), may hold values from -6 to 6
- ln_gain: float32 [512], replicated, may hold values from 0.25 to 1.75
- w_qkv: bfloat16 [512, 1536], replicated, may hold values from -1 to 1
- w_out: bfloat16 [512, 512], replicated, may hold values from -0.25 to 0.25
Outputs:
- grad_x: bfloat16 [2, 256, 256, 512], P(None, 'gx', 'gy')
- grad_wqkv: float32 [512, 1536], replicated
- grad_wout: float32 [512, 512], replicated
- grad_gain: float32 [512], replicated
The draws below stay inside these ranges and needn't reach their ends.
All inputs are finite; a program needn't handle non-finite values.
Results may differ from the reference program's by a relative error of at most 0.0028.
The reference program's roundings to bfloat16 on the way count: a program that leaves them out, or rounds other values in their place, can miss the bound.
Values may be sent and summed in bfloat16 or wider, within the bound.
No kernel may reach another device: no remote copies, remote signals or barrier semaphores. Data moves between devices by JAX's collectives and lax.ppermute only.
A program may use at most 128 MiB of HBM per device.

```python
import math
import jax
import jax.numpy as jnp
from jax import lax

WIDTH = 512
HEADS = 8
GRID = 16
FRAMES = 2
HEAD_DIM = 64
MAP_H = 256
MAP_W = 256
STRIDE_H = 16
STRIDE_W = 16
TOKENS = 131072


def draw_tokens_in(key, part):
    shape = (FRAMES, MAP_H, MAP_W, WIDTH)
    noise = jnp.clip(jax.random.normal(jax.random.fold_in(key, 1), shape, jnp.float32), -4.0, 4.0)
    row_scale = jnp.exp(jax.random.uniform(jax.random.fold_in(key, 2), (FRAMES, MAP_H, MAP_W, 1), jnp.float32, math.log(0.4), math.log(4.0)))
    col_scale = jnp.exp(jax.random.uniform(jax.random.fold_in(key, 3), (WIDTH,), jnp.float32, math.log(0.4), math.log(4.0)))
    result = noise * col_scale * row_scale
    return result.astype(jnp.bfloat16)


def draw_w_qkv(key, part):
    base = jnp.clip(jax.random.normal(jax.random.fold_in(key, 11), (WIDTH, 3 * WIDTH), jnp.float32), -5.0, 5.0)
    base = base / math.sqrt(WIDTH)
    result = base
    return result.astype(jnp.bfloat16)


def shard_levels(rng, shape, pieces, least, high):
    def one(dim, blocks):
        steps = jax.random.uniform(jax.random.fold_in(jax.random.fold_in(rng, 6), dim), (blocks,), jnp.float32, least / len(pieces), high / len(pieces))
        return jnp.repeat(jnp.exp(steps), shape[dim] // blocks).reshape((-1,) + (1,) * (len(shape) - dim - 1))

    level = one(*pieces[0])
    for cut in pieces[1:]:
        level = level * one(*cut)
    return level


def bell_draw(rng, shape, spread, most, cuts=(), dtype=jnp.bfloat16):
    array = jax.random.normal(rng, shape, jnp.float32) * spread
    if len(cuts) > 0:
        array = shard_levels(rng, shape, cuts, -0.22, 0.18) * array
    return jnp.clip(array, min=-most, max=most).astype(dtype)


def setup_inputs(seed: int = 0) -> dict:
    key_of = jax.random.split(jax.random.key(seed), 6)
    return {
        "tokens_in": draw_tokens_in(jax.random.fold_in(key_of[5], 71), 0),
        "grad_out": bell_draw(key_of[1], (FRAMES, MAP_H, MAP_W, WIDTH), 1.0, 6.0, ((1, 16), (2, 8))),
        "ln_gain": jnp.clip(1.0 + 0.15 * jax.random.normal(key_of[2], (WIDTH,), jnp.float32), 0.25, 1.75),
        "w_qkv": draw_w_qkv(jax.random.fold_in(key_of[5], 71), 0),
        "w_out": bell_draw(key_of[4], (WIDTH, WIDTH), WIDTH ** -0.5, 0.25),
    }


def round_half(values):
    return lax.optimization_barrier(values.astype(jnp.bfloat16))

def norm_parts(values):
    center = values - lax.optimization_barrier(jnp.mean(values, axis=-1, keepdims=True))
    variance = lax.optimization_barrier(jnp.mean(center * center, axis=-1, keepdims=True))
    inv_std = lax.rsqrt(variance + 1e-05)
    return (center * inv_std, inv_std)

def regroup(frame):
    channels = frame.shape[-1]
    shaped = frame.reshape(GRID, STRIDE_H, GRID, STRIDE_W, channels)
    return shaped.transpose(1, 3, 0, 2, 4).reshape(STRIDE_H * STRIDE_W, GRID * GRID, channels)

def ungroup(grouped):
    channels = grouped.shape[-1]
    shaped = grouped.reshape(STRIDE_H, STRIDE_W, GRID, GRID, channels)
    return shaped.transpose(2, 0, 3, 1, 4).reshape(MAP_H * MAP_W, channels)

def attend_block(pair):
    qkv_part, dout_part = pair
    scale = 1.0 / math.sqrt(HEAD_DIM)
    hp = lax.Precision.HIGHEST
    part = qkv_part.astype(jnp.float32)
    query = part[:, :, 0]
    key = part[:, :, 1]
    value = part[:, :, 2]
    dout = dout_part.astype(jnp.float32)
    scores = jnp.einsum('bqhd,bkhd->bhqk', query, key, precision=hp) * scale
    top = lax.optimization_barrier(jnp.max(scores, axis=-1, keepdims=True))
    expd = jnp.exp(scores - top)
    probs = expd / lax.optimization_barrier(jnp.sum(expd, axis=-1, keepdims=True))
    probs_b = round_half(probs).astype(jnp.float32)
    attn = round_half(jnp.einsum('bhqk,bkhd->bqhd', probs_b, value, precision=hp))
    grad_value = round_half(jnp.einsum('bhqk,bqhd->bkhd', probs_b, dout, precision=hp))
    grad_probs = jnp.einsum('bqhd,bkhd->bhqk', dout, value, precision=hp)
    inner = lax.optimization_barrier(jnp.sum(probs * grad_probs, axis=-1, keepdims=True))
    grad_scores = round_half(probs * (grad_probs - inner) * scale).astype(jnp.float32)
    grad_query = round_half(jnp.einsum('bhqk,bkhd->bqhd', grad_scores, key, precision=hp))
    grad_key = round_half(jnp.einsum('bhqk,bqhd->bkhd', grad_scores, query, precision=hp))
    return (attn, jnp.stack([grad_query, grad_key, grad_value], axis=2))

def grid_attention(qkv_groups, dout_groups):
    count = qkv_groups.shape[0]
    members = qkv_groups.shape[1]
    block = 2 if count % 2 == 0 else 1
    qkv_blocks = qkv_groups.reshape(count // block, block, members, 3, HEADS, HEAD_DIM)
    dout_blocks = dout_groups.reshape(count // block, block, members, HEADS, HEAD_DIM)
    attn, grads = lax.map(attend_block, (qkv_blocks, dout_blocks))
    return (attn.reshape(count, members, WIDTH), grads.reshape(count, members, 3 * WIDTH))

def reference(tokens_in, grad_out, ln_gain, w_qkv, w_out):

    def frame_step(carry, pair):
        sum_wqkv, sum_wout, sum_gain = carry
        frame_in, frame_grad = pair
        flat_in = frame_in.reshape(-1, WIDTH)
        flat_grad = frame_grad.reshape(-1, WIDTH)
        normed, inv_std = norm_parts(flat_in.astype(jnp.float32))
        hidden = (normed * ln_gain).astype(jnp.bfloat16)
        qkv = jnp.dot(hidden, w_qkv, preferred_element_type=jnp.float32).astype(jnp.bfloat16)
        grad_attn = jnp.dot(flat_grad, w_out.T, preferred_element_type=jnp.float32).astype(jnp.bfloat16)
        attn_g, grad_g = grid_attention(regroup(qkv.reshape(MAP_H, MAP_W, 3 * WIDTH)), regroup(grad_attn.reshape(MAP_H, MAP_W, WIDTH)))
        attn = ungroup(attn_g)
        grad_qkv = ungroup(grad_g)
        grad_hidden = jnp.dot(grad_qkv, w_qkv.T, preferred_element_type=jnp.float32)
        sum_wout = sum_wout + jnp.dot(attn.T, flat_grad, preferred_element_type=jnp.float32)
        sum_wqkv = sum_wqkv + jnp.dot(hidden.T, grad_qkv, preferred_element_type=jnp.float32)
        sum_gain = sum_gain + lax.optimization_barrier(jnp.sum(normed * grad_hidden, axis=0))
        scaled = grad_hidden * ln_gain
        branch = inv_std * (scaled - lax.optimization_barrier(jnp.mean(scaled, axis=-1, keepdims=True)) - normed * lax.optimization_barrier(jnp.mean(scaled * normed, axis=-1, keepdims=True)))
        branch = round_half(branch).astype(jnp.float32)
        result = (flat_grad.astype(jnp.float32) + branch).astype(jnp.bfloat16)
        return ((sum_wqkv, sum_wout, sum_gain), result.reshape(MAP_H, MAP_W, WIDTH))
    start = (jnp.zeros((WIDTH, 3 * WIDTH), jnp.float32), jnp.zeros((WIDTH, WIDTH), jnp.float32), jnp.zeros((WIDTH,), jnp.float32))
    sums, grad_x = lax.scan(frame_step, start, (tokens_in, grad_out))
    factor = 1.0 / math.sqrt(TOKENS)
    return (grad_x, sums[0] * factor, sums[1] * factor, sums[2] * factor)
```

```python
import math

import jax
import jax.numpy as jnp
from jax import lax
from jax.sharding import Mesh, PartitionSpec as P

HEADS = 8
GRID = 16
HEAD_DIM = 64
ALL = ("gxc", "core", "gy")
CHIPS = ("gxc", "gy")


def swap_core(values):
    return lax.ppermute(values, "core", [(0, 1), (1, 0)])


def reduce_all(weights, gain):
    rows, width = weights.shape
    chips = lax.axis_size("gxc") * lax.axis_size("gy")
    core = lax.axis_index("core")
    half = rows // 2
    ghalf = gain.shape[0] // 2
    mine = lax.dynamic_slice_in_dim(weights, core * half, half, 0)
    other = lax.dynamic_slice_in_dim(weights, (1 - core) * half, half, 0)
    gmine = lax.dynamic_slice_in_dim(gain, core * ghalf, ghalf, 0)
    gother = lax.dynamic_slice_in_dim(gain, (1 - core) * ghalf, ghalf, 0)
    got, ggot = swap_core((other, gother))
    part_w = (mine + got).reshape(chips, -1)
    part_g = (gmine + ggot).reshape(chips, -1)
    pad = 128 - part_g.shape[1]
    packed = jnp.concatenate([part_w, part_g, jnp.zeros((chips, pad), jnp.float32)], axis=1)
    summed = lax.all_to_all(packed, CHIPS, 0, 0, tiled=True).sum(0)
    spread = jnp.broadcast_to(summed[None], (chips,) + summed.shape)
    gathered = lax.all_to_all(spread, CHIPS, 0, 0, tiled=True)
    own_w = gathered[:, : part_w.shape[1]].reshape(half, width)
    own_g = gathered[:, part_w.shape[1] : part_w.shape[1] + part_g.shape[1]].reshape(ghalf)
    peer_w, peer_g = swap_core((own_w, own_g))
    first = core == 0
    full_w = jnp.where(first, jnp.concatenate([own_w, peer_w], 0), jnp.concatenate([peer_w, own_w], 0))
    full_g = jnp.where(first, jnp.concatenate([own_g, peer_g], 0), jnp.concatenate([peer_g, own_g], 0))
    return full_w, full_g


def to_groups(values, grid_rows, grid_cols):
    frames, tile_rows, tile_cols, channels = values.shape
    stride_rows = tile_rows // grid_rows
    stride_cols = tile_cols // grid_cols
    shaped = values.reshape(frames, grid_rows, stride_rows, grid_cols, stride_cols, channels)
    shaped = shaped.transpose(0, 2, 4, 1, 3, 5)
    return shaped.reshape(frames * stride_rows * stride_cols, grid_rows * grid_cols, channels)


def from_groups(grouped, frames, grid_rows, grid_cols, stride_rows, stride_cols):
    channels = grouped.shape[-1]
    shaped = grouped.reshape(frames, stride_rows, stride_cols, grid_rows, grid_cols, channels)
    shaped = shaped.transpose(0, 3, 1, 4, 2, 5)
    return shaped.reshape(frames, grid_rows * stride_rows, grid_cols * stride_cols, channels)


def attend_block(pair):
    qkv_part, dout = pair
    scale = 1.0 / math.sqrt(HEAD_DIM)
    query = qkv_part[:, :, 0]
    key = qkv_part[:, :, 1]
    value = qkv_part[:, :, 2]
    scores = jnp.einsum("bqhd,bkhd->bhqk", query, key, preferred_element_type=jnp.float32) * scale
    top = jnp.max(scores, axis=-1, keepdims=True)
    expd = jnp.exp(scores - top)
    probs = expd / jnp.sum(expd, axis=-1, keepdims=True)
    probs_b = probs.astype(jnp.bfloat16)
    attn = jnp.einsum("bhqk,bkhd->bqhd", probs_b, value, preferred_element_type=jnp.float32).astype(
        jnp.bfloat16
    )
    grad_value = jnp.einsum(
        "bhqk,bqhd->bkhd", probs_b, dout, preferred_element_type=jnp.float32
    ).astype(jnp.bfloat16)
    grad_probs = jnp.einsum("bqhd,bkhd->bhqk", dout, value, preferred_element_type=jnp.float32)
    inner = jnp.sum(probs * grad_probs, axis=-1, keepdims=True)
    grad_scores = (probs * (grad_probs - inner) * scale).astype(jnp.bfloat16)
    grad_query = jnp.einsum(
        "bhqk,bkhd->bqhd", grad_scores, key, preferred_element_type=jnp.float32
    ).astype(jnp.bfloat16)
    grad_key = jnp.einsum(
        "bhqk,bqhd->bkhd", grad_scores, query, preferred_element_type=jnp.float32
    ).astype(jnp.bfloat16)
    return (attn, jnp.stack([grad_query, grad_key, grad_value], axis=2))


def local(tokens_in, grad_out, ln_gain, w_qkv, w_out):
    count_x = lax.axis_size("gxc") * lax.axis_size("core")
    count_y = lax.axis_size("gy")
    frames, tile_rows, tile_cols, channels = tokens_in.shape
    grid_rows = GRID // count_x
    grid_cols = GRID // count_y
    stride_rows = tile_rows // grid_rows
    stride_cols = tile_cols // grid_cols
    total_tokens = frames * tile_rows * tile_cols * count_x * count_y
    grouped_in = to_groups(tokens_in, grid_rows, grid_cols)
    grouped_grad = to_groups(grad_out, grid_rows, grid_cols)
    moved_in, moved_grad = (
        lax.all_to_all(grouped_in, ALL, split_axis=0, concat_axis=1, tiled=True),
        lax.all_to_all(grouped_grad, ALL, split_axis=0, concat_axis=1, tiled=True),
    )
    owned = moved_in.shape[0]
    members = moved_in.shape[1]
    flat_in = moved_in.reshape(-1, channels)
    flat_grad = moved_grad.reshape(-1, channels)
    values = flat_in.astype(jnp.float32)
    center = values - jnp.mean(values, axis=-1, keepdims=True)
    inv_std = lax.rsqrt(jnp.mean(center * center, axis=-1, keepdims=True) + 1e-05)
    normed = center * inv_std
    hidden = (normed * ln_gain).astype(jnp.bfloat16)
    qkv = jnp.dot(hidden, w_qkv, preferred_element_type=jnp.float32).astype(jnp.bfloat16)
    grad_attn = lax.dot_general(
        flat_grad, w_out, (((1,), (1,)), ((), ())), preferred_element_type=jnp.float32
    ).astype(jnp.bfloat16)
    block = 2
    qkv_blocks = qkv.reshape(owned // block, block, members, 3, HEADS, HEAD_DIM)
    dout_blocks = grad_attn.reshape(owned // block, block, members, HEADS, HEAD_DIM)
    attn_blocks, grad_blocks = lax.map(attend_block, (qkv_blocks, dout_blocks))
    attn = attn_blocks.reshape(-1, channels)
    grad_qkv = grad_blocks.reshape(-1, 3 * channels)
    local_wout = lax.dot_general(
        attn, flat_grad, (((0,), (0,)), ((), ())), preferred_element_type=jnp.float32
    )
    grad_hidden = lax.dot_general(
        grad_qkv, w_qkv, (((1,), (1,)), ((), ())), preferred_element_type=jnp.float32
    )
    scaled = grad_hidden * ln_gain
    branch = inv_std * (
        scaled
        - jnp.mean(scaled, axis=-1, keepdims=True)
        - normed * jnp.mean(scaled * normed, axis=-1, keepdims=True)
    )
    branch = branch.astype(jnp.bfloat16).reshape(owned, members, channels)
    returned = lax.all_to_all(branch, ALL, split_axis=1, concat_axis=0, tiled=True)
    local_wqkv = lax.dot_general(
        hidden, grad_qkv, (((0,), (0,)), ((), ())), preferred_element_type=jnp.float32
    )
    local_gain = jnp.sum(normed * grad_hidden, axis=0)
    summed_w, summed_gain = reduce_all(
        jnp.concatenate([local_wqkv, local_wout], axis=1), local_gain
    )
    summed_wqkv = summed_w[:, : local_wqkv.shape[1]]
    summed_wout = summed_w[:, local_wqkv.shape[1] :]
    tiled = from_groups(returned, frames, grid_rows, grid_cols, stride_rows, stride_cols)
    grad_x = (grad_out.astype(jnp.float32) + tiled.astype(jnp.float32)).astype(jnp.bfloat16)
    factor = 1.0 / math.sqrt(total_tokens)
    return (grad_x, summed_wqkv * factor, summed_wout * factor, summed_gain * factor)


def solution(mesh):
    rows, cols = mesh.devices.shape
    split = Mesh(mesh.devices.reshape(rows // 2, 2, cols), ("gxc", "core", "gy"))
    tile = P(None, ("gxc", "core"), "gy", None)
    in_specs = (tile, tile, P(), P(), P())
    out_specs = (tile, P(), P(), P())
    return jax.shard_map(local, mesh=split, in_specs=in_specs, out_specs=out_specs, check_vma=False)
```

```python
import math

import jax
import jax.numpy as jnp
from jax import lax
from jax.experimental import pallas as pl
from jax.sharding import Mesh, PartitionSpec as P

HEADS = 8
GRID = 16
HEAD_DIM = 64
ALL = ("gxc", "core", "gy")
CHIPS = ("gxc", "gy")


def swap_core(values):
    return lax.ppermute(values, "core", [(0, 1), (1, 0)])


def reduce_all(weights, gain):
    rows, width = weights.shape
    chips = lax.axis_size("gxc") * lax.axis_size("gy")
    core = lax.axis_index("core")
    half = rows // 2
    ghalf = gain.shape[0] // 2
    mine = lax.dynamic_slice_in_dim(weights, core * half, half, 0)
    other = lax.dynamic_slice_in_dim(weights, (1 - core) * half, half, 0)
    gmine = lax.dynamic_slice_in_dim(gain, core * ghalf, ghalf, 0)
    gother = lax.dynamic_slice_in_dim(gain, (1 - core) * ghalf, ghalf, 0)
    got, ggot = swap_core((other, gother))
    part_w = (mine + got).reshape(chips, -1)
    part_g = (gmine + ggot).reshape(chips, -1)
    pad = 128 - part_g.shape[1]
    packed = jnp.concatenate([part_w, part_g, jnp.zeros((chips, pad), jnp.float32)], axis=1)
    summed = lax.all_to_all(packed, CHIPS, 0, 0, tiled=True).sum(0)
    spread = jnp.broadcast_to(summed[None], (chips,) + summed.shape)
    gathered = lax.all_to_all(spread, CHIPS, 0, 0, tiled=True)
    own_w = gathered[:, : part_w.shape[1]].reshape(half, width)
    own_g = gathered[:, part_w.shape[1] : part_w.shape[1] + part_g.shape[1]].reshape(ghalf)
    peer_w, peer_g = swap_core((own_w, own_g))
    first = core == 0
    full_w = jnp.where(first, jnp.concatenate([own_w, peer_w], 0), jnp.concatenate([peer_w, own_w], 0))
    full_g = jnp.where(first, jnp.concatenate([own_g, peer_g], 0), jnp.concatenate([peer_g, own_g], 0))
    return full_w, full_g


def to_groups(values, grid_rows, grid_cols):
    frames, tile_rows, tile_cols, channels = values.shape
    stride_rows = tile_rows // grid_rows
    stride_cols = tile_cols // grid_cols
    shaped = values.reshape(frames, grid_rows, stride_rows, grid_cols, stride_cols, channels)
    shaped = shaped.transpose(0, 2, 4, 1, 3, 5)
    return shaped.reshape(frames * stride_rows * stride_cols, grid_rows * grid_cols, channels)


def from_groups(grouped, frames, grid_rows, grid_cols, stride_rows, stride_cols):
    channels = grouped.shape[-1]
    shaped = grouped.reshape(frames, stride_rows, stride_cols, grid_rows, grid_cols, channels)
    shaped = shaped.transpose(0, 3, 1, 4, 2, 5)
    return shaped.reshape(frames, grid_rows * stride_rows, grid_cols * stride_cols, channels)


def attention_kernel(qkv_ref, dout_ref, attn_ref, grad_ref):
    scale = 1.0 / math.sqrt(HEAD_DIM)
    width = HEADS * HEAD_DIM
    members = qkv_ref.shape[1]
    lanes = 2 * HEAD_DIM
    first = lax.broadcasted_iota(jnp.int32, (members, lanes), 1) < HEAD_DIM
    nt = (((1,), (1,)), ((), ()))
    tn = (((0,), (0,)), ((), ()))
    for pair in range(HEADS // 2):
        cols = slice(pair * lanes, (pair + 1) * lanes)
        query = qkv_ref[0, :, pair * lanes : (pair + 1) * lanes]
        key = qkv_ref[0, :, width + pair * lanes : width + (pair + 1) * lanes]
        value = qkv_ref[0, :, 2 * width + pair * lanes : 2 * width + (pair + 1) * lanes]
        dout = dout_ref[0, :, cols]
        outs = []
        for sel in (first, jnp.logical_not(first)):
            zero = jnp.zeros_like(query)
            q_h = jnp.where(sel, query, zero)
            scores = lax.dot_general(q_h, key, nt, preferred_element_type=jnp.float32) * scale
            top = jnp.max(scores, axis=-1, keepdims=True)
            expd = jnp.exp(scores - top)
            probs = expd / jnp.sum(expd, axis=-1, keepdims=True)
            probs_b = probs.astype(jnp.bfloat16)
            attn = jnp.dot(probs_b, value, preferred_element_type=jnp.float32)
            grad_value = lax.dot_general(probs_b, dout, tn, preferred_element_type=jnp.float32)
            d_h = jnp.where(sel, dout, zero)
            grad_probs = lax.dot_general(d_h, value, nt, preferred_element_type=jnp.float32)
            inner = jnp.sum(probs * grad_probs, axis=-1, keepdims=True)
            grad_scores = (probs * (grad_probs - inner) * scale).astype(jnp.bfloat16)
            grad_query = jnp.dot(grad_scores, key, preferred_element_type=jnp.float32)
            grad_key = lax.dot_general(grad_scores, query, tn, preferred_element_type=jnp.float32)
            outs.append(
                tuple(x.astype(jnp.bfloat16) for x in (attn, grad_query, grad_key, grad_value))
            )
        (a0, q0, k0, v0), (a1, q1, k1, v1) = outs
        attn_ref[0, :, cols] = jnp.where(first, a0, a1)
        grad_ref[0, :, pair * lanes : (pair + 1) * lanes] = jnp.where(first, q0, q1)
        grad_ref[0, :, width + pair * lanes : width + (pair + 1) * lanes] = jnp.where(first, k0, k1)
        grad_ref[0, :, 2 * width + pair * lanes : 2 * width + (pair + 1) * lanes] = jnp.where(first, v0, v1)


def grid_attention(qkv, dout):
    groups, members, three = qkv.shape
    width = dout.shape[-1]
    return pl.pallas_call(
        attention_kernel,
        grid=(groups,),
        in_specs=[
            pl.BlockSpec((1, members, three), lambda g: (g, 0, 0)),
            pl.BlockSpec((1, members, width), lambda g: (g, 0, 0)),
        ],
        out_specs=[
            pl.BlockSpec((1, members, width), lambda g: (g, 0, 0)),
            pl.BlockSpec((1, members, three), lambda g: (g, 0, 0)),
        ],
        out_shape=[
            jax.ShapeDtypeStruct((groups, members, width), jnp.bfloat16),
            jax.ShapeDtypeStruct((groups, members, three), jnp.bfloat16),
        ],
    )(qkv, dout)


def local(tokens_in, grad_out, ln_gain, w_qkv, w_out):
    count_x = lax.axis_size("gxc") * lax.axis_size("core")
    count_y = lax.axis_size("gy")
    frames, tile_rows, tile_cols, channels = tokens_in.shape
    grid_rows = GRID // count_x
    grid_cols = GRID // count_y
    stride_rows = tile_rows // grid_rows
    stride_cols = tile_cols // grid_cols
    total_tokens = frames * tile_rows * tile_cols * count_x * count_y
    grouped_in = to_groups(tokens_in, grid_rows, grid_cols)
    grouped_grad = to_groups(grad_out, grid_rows, grid_cols)
    moved_in, moved_grad = (
        lax.all_to_all(grouped_in, ALL, split_axis=0, concat_axis=1, tiled=True),
        lax.all_to_all(grouped_grad, ALL, split_axis=0, concat_axis=1, tiled=True),
    )
    owned = moved_in.shape[0]
    members = moved_in.shape[1]
    flat_in = moved_in.reshape(-1, channels)
    flat_grad = moved_grad.reshape(-1, channels)
    values = flat_in.astype(jnp.float32)
    center = values - jnp.mean(values, axis=-1, keepdims=True)
    inv_std = lax.rsqrt(jnp.mean(center * center, axis=-1, keepdims=True) + 1e-05)
    normed = center * inv_std
    hidden = (normed * ln_gain).astype(jnp.bfloat16)
    qkv = jnp.dot(hidden, w_qkv, preferred_element_type=jnp.float32).astype(jnp.bfloat16)
    grad_attn = lax.dot_general(
        flat_grad, w_out, (((1,), (1,)), ((), ())), preferred_element_type=jnp.float32
    ).astype(jnp.bfloat16)
    attn_groups, grad_groups = grid_attention(
        qkv.reshape(owned, members, 3 * channels), grad_attn.reshape(owned, members, channels)
    )
    attn = attn_groups.reshape(-1, channels)
    grad_qkv = grad_groups.reshape(-1, 3 * channels)
    local_wout = lax.dot_general(
        attn, flat_grad, (((0,), (0,)), ((), ())), preferred_element_type=jnp.float32
    )
    grad_hidden = lax.dot_general(
        grad_qkv, w_qkv, (((1,), (1,)), ((), ())), preferred_element_type=jnp.float32
    )
    scaled = grad_hidden * ln_gain
    branch = inv_std * (
        scaled
        - jnp.mean(scaled, axis=-1, keepdims=True)
        - normed * jnp.mean(scaled * normed, axis=-1, keepdims=True)
    )
    branch = branch.astype(jnp.bfloat16).reshape(owned, members, channels)
    returned = lax.all_to_all(branch, ALL, split_axis=1, concat_axis=0, tiled=True)
    local_wqkv = lax.dot_general(
        hidden, grad_qkv, (((0,), (0,)), ((), ())), preferred_element_type=jnp.float32
    )
    local_gain = jnp.sum(normed * grad_hidden, axis=0)
    summed_w, summed_gain = reduce_all(
        jnp.concatenate([local_wqkv, local_wout], axis=1), local_gain
    )
    summed_wqkv = summed_w[:, : local_wqkv.shape[1]]
    summed_wout = summed_w[:, local_wqkv.shape[1] :]
    tiled = from_groups(returned, frames, grid_rows, grid_cols, stride_rows, stride_cols)
    grad_x = (grad_out.astype(jnp.float32) + tiled.astype(jnp.float32)).astype(jnp.bfloat16)
    factor = 1.0 / math.sqrt(total_tokens)
    return (grad_x, summed_wqkv * factor, summed_wout * factor, summed_gain * factor)


def solution(mesh):
    rows, cols = mesh.devices.shape
    split = Mesh(mesh.devices.reshape(rows // 2, 2, cols), ("gxc", "core", "gy"))
    tile = P(None, ("gxc", "core"), "gy", None)
    in_specs = (tile, tile, P(), P(), P())
    out_specs = (tile, P(), P(), P())
    return jax.shard_map(local, mesh=split, in_specs=in_specs, out_specs=out_specs, check_vma=False)
```
